32 devices in a mesh: grp: 4 (over z), seq: 8 (over y, x, core).
Axes of the slice: x: 2, y: 2, z: 4, core: 2. Of those that a mesh axis runs over, the one named last changes fastest.
Arguments:
- queries: bfloat16 [32768, 1024], P(('grp', 'seq')), may hold values from -6 to 6
- keys: bfloat16 [32768, 1024], P(('grp', 'seq')), may hold values from -6 to 6
- values: bfloat16 [32768, 1024], P(('grp', 'seq')), may hold values from -4 to 4
- cache_kv: bfloat16 [2, 128, 1024, 512], P(None, 'grp', 'seq'), may hold values from -4 to 4
- thread_start: int32 [32], replicated, may hold values from 1024 to 162816, as said below
Outputs:
- attended: bfloat16 [32768, 1024], P(('grp', 'seq'))
The draws below stay inside these ranges and needn't reach their ends.
Inputs may be any that keep to these rules, and one draw needn't show every extreme that they name: `thread_start`: Non-decreasing multiples of 1024; rows with equal entries are consecutive and form one thread. The first window rows belong to a thread that began inside the cache: their entry is s * 1024 for a cached context row s with 1 <= s <= 64. Every later thread begins at a window row b > 0, and its entry is (128 + b) * 1024; the last row begins a thread of its own.
All inputs are finite; a program needn't handle non-finite values.
Results may differ from the reference program's by a relative error of at most 0.0028.
Values may be sent and summed in bfloat16 or wider, within the bound.
No kernel may reach another device: no remote copies, remote signals or barrier semaphores. Data moves between devices by JAX's collectives and lax.ppermute only.
A program may use at most 256 MiB of HBM per device.

```python
import jax
import jax.numpy as jnp
from jax import lax

LH = 8
SH = 8
HD = 64
STRIDE = 1024
CACHE = 128
ROWS = 32
TOKENS = 32768


def drawn_base(key, tag):
    width = (LH + SH) * HD
    return jnp.clip(jax.random.normal(jax.random.fold_in(key, tag), (TOKENS, width), jnp.float32), -4.0, 4.0)


def draw_queries(key, part):
    return drawn_base(key, 11).astype(jnp.bfloat16)


def draw_keys(key, part):
    return drawn_base(key, 21).astype(jnp.bfloat16)


def draw_thread_start(key, part):
    index = jnp.arange(ROWS, dtype=jnp.int32)
    begins = jax.random.randint(jax.random.fold_in(key, 31), (ROWS,), 0, 16) == 0
    begins = begins & (index > 0) | (index == ROWS - 1)
    opening = jax.random.randint(jax.random.fold_in(key, 32), (), 1, CACHE // 2 + 1).astype(jnp.int32)
    first_row = jnp.where(begins, CACHE + index, opening).astype(jnp.int32)
    return (lax.cummax(first_row, axis=0) * STRIDE).astype(jnp.int32)


def levels(own_key, dims, shards, low, high):
    level = 1.0
    for axis_at, blocks in shards:
        draws = jax.random.uniform(jax.random.fold_in(jax.random.fold_in(own_key, 6), axis_at), (blocks,), jnp.float32, low / len(shards), high / len(shards))
        level = level * jnp.repeat(jnp.exp(draws), dims[axis_at] // blocks).reshape((-1,) + (1,) * (len(dims) - 1 - axis_at))
    return level


def normal_values(rng, shape, deviation, most, shards=(), kind=jnp.bfloat16):
    level = levels(rng, shape, shards, -0.22, 0.18) if shards else 1.0
    entries = jax.random.normal(rng, shape, jnp.float32) * deviation * level
    return jnp.minimum(jnp.maximum(entries, -most), most).astype(kind)


def setup_inputs(seed: int = 0) -> dict:
    seeds = jax.random.split(jax.random.key(seed), 6)
    queries = draw_queries(jax.random.fold_in(seeds[5], 71), 0)
    keys = draw_keys(jax.random.fold_in(seeds[5], 71), 0)
    values = normal_values(seeds[2], (TOKENS, (LH + SH) * HD), 1.0, 4.0, ((0, 32),))
    cache_kv = normal_values(seeds[3], (2, CACHE, STRIDE, SH * HD), 1.0, 4.0, ((1, 4), (2, 8)))
    thread_start = draw_thread_start(jax.random.fold_in(seeds[5], 71), 0)
    return dict(queries=queries, keys=keys, values=values, cache_kv=cache_kv, thread_start=thread_start)


def reference(queries, keys, values, cache_kv, thread_start):
    scale = HD ** -0.5
    width_l = LH * HD
    width_s = SH * HD
    q_loc = queries[:, :width_l].reshape(ROWS, STRIDE, LH, HD)
    k_loc = keys[:, :width_l].reshape(ROWS, STRIDE, LH, HD)
    v_loc = values[:, :width_l].reshape(ROWS, STRIDE, LH, HD)
    place = jnp.arange(STRIDE, dtype=jnp.int32)
    causal = place[:, None] >= place[None, :]

    def local_row(parts):
        q, k, v = parts
        scores = jnp.einsum('qhd,khd->hqk', q.astype(jnp.float32), k.astype(jnp.float32)) * scale
        scores = jnp.where(causal[None], scores, -jnp.inf)
        top = jnp.max(scores, axis=-1, keepdims=True)
        expo = jnp.exp(scores - top)
        total = jnp.sum(expo, axis=-1)
        weights = expo.astype(jnp.bfloat16).astype(jnp.float32)
        mixed = jnp.einsum('hqk,khd->qhd', weights, v.astype(jnp.float32))
        return mixed / jnp.transpose(total)[:, :, None]

    local_out = lax.map(local_row, (q_loc, k_loc, v_loc)).reshape(TOKENS, width_l)

    q_str = queries[:, width_l:].reshape(ROWS, STRIDE, SH, HD).transpose(1, 0, 2, 3)
    k_str = jnp.concatenate([cache_kv[0].reshape(CACHE, STRIDE, SH, HD),
                             keys[:, width_l:].reshape(ROWS, STRIDE, SH, HD)], axis=0).transpose(1, 0, 2, 3)
    v_str = jnp.concatenate([cache_kv[1].reshape(CACHE, STRIDE, SH, HD),
                             values[:, width_l:].reshape(ROWS, STRIDE, SH, HD)], axis=0).transpose(1, 0, 2, 3)
    start_row = thread_start // STRIDE
    key_rows = jnp.arange(CACHE + ROWS, dtype=jnp.int32)
    query_rows = CACHE + jnp.arange(ROWS, dtype=jnp.int32)
    visible = (key_rows[None, :] >= start_row[:, None]) & (key_rows[None, :] <= query_rows[:, None])
    block = min(32, STRIDE)
    count = STRIDE // block

    def column_block(parts):
        q, k, v = parts
        scores = jnp.einsum('crhd,cmhd->chrm', q.astype(jnp.float32), k.astype(jnp.float32)) * scale
        scores = jnp.where(visible[None, None], scores, -jnp.inf)
        top = jnp.max(scores, axis=-1, keepdims=True)
        expo = jnp.exp(scores - top)
        total = jnp.sum(expo, axis=-1)
        weights = expo.astype(jnp.bfloat16).astype(jnp.float32)
        mixed = jnp.einsum('chrm,cmhd->crhd', weights, v.astype(jnp.float32))
        return mixed / jnp.transpose(total, (0, 2, 1))[..., None]

    strided = lax.map(column_block, (q_str.reshape(count, block, ROWS, SH, HD),
                                     k_str.reshape(count, block, CACHE + ROWS, SH, HD),
                                     v_str.reshape(count, block, CACHE + ROWS, SH, HD)))
    strided_out = strided.reshape(STRIDE, ROWS, SH, HD).transpose(1, 0, 2, 3).reshape(TOKENS, width_s)
    return jnp.concatenate([local_out, strided_out], axis=1).astype(jnp.bfloat16)
```

```python
import jax
import jax.numpy as jnp
from jax import lax
from jax.sharding import PartitionSpec as P

LH = 8
SH = 8
HD = 64
STRIDE = 1024
CACHE = 128


def local_attention(q_part, k_part, v_part):
    scale = HD ** (-0.5)
    tok = q_part.shape[0]
    rows_dev = tok // STRIDE
    block = min(512, STRIDE)
    per_row = STRIDE // block
    q_blocks = q_part.reshape(tok // block, block, LH, HD)
    k_rows = k_part.reshape(rows_dev, STRIDE, LH, HD)
    v_rows = v_part.reshape(rows_dev, STRIDE, LH, HD)
    key_place = jnp.arange(STRIDE, dtype=jnp.int32)

    def one_block(index):
        row_index = index // per_row
        first = index % per_row * block
        query = lax.dynamic_index_in_dim(q_blocks, index, 0, keepdims=False)
        key_row = lax.dynamic_index_in_dim(k_rows, row_index, 0, keepdims=False)
        value_row = lax.dynamic_index_in_dim(v_rows, row_index, 0, keepdims=False)
        scores = (
            jnp.einsum("qhd,khd->hqk", query, key_row, preferred_element_type=jnp.float32) * scale
        )
        causal = (first + jnp.arange(block, dtype=jnp.int32))[:, None] >= key_place[None, :]
        scores = jnp.where(causal[None], scores, -jnp.inf)
        top = jnp.max(scores, axis=-1, keepdims=True)
        expo = jnp.exp(scores - top)
        total = jnp.sum(expo, axis=-1)
        mixed = jnp.einsum(
            "hqk,khd->qhd", expo.astype(jnp.bfloat16), value_row, preferred_element_type=jnp.float32
        )
        return (mixed / jnp.transpose(total)[:, :, None]).reshape(block, LH * HD)

    result = lax.map(one_block, jnp.arange(tok // block, dtype=jnp.int32))
    return result.reshape(tok, LH * HD)


def strided_attention(queries, keys, values, cache_kv, thread_start):
    scale = HD ** (-0.5)
    width_l = LH * HD
    width_s = SH * HD
    tok = queries.shape[0]
    rows_dev = tok // STRIDE
    cache_here = cache_kv.shape[1]
    cols_here = cache_kv.shape[2]
    rows_all = thread_start.shape[0]
    grp = lax.axis_index("grp")

    own_q = queries[:, width_l:].reshape(rows_dev, STRIDE, width_s)
    own_kv = jnp.stack([keys[:, width_l:], values[:, width_l:]]).reshape(2, rows_dev, STRIDE, width_s)
    plane_q = lax.all_to_all(own_q, "seq", split_axis=1, concat_axis=0, tiled=True)
    plane_kv = lax.all_to_all(own_kv, "seq", split_axis=2, concat_axis=1, tiled=True)
    rows_plane = plane_q.shape[0]
    all_q = lax.all_gather(plane_q, "grp", axis=0, tiled=True)

    k_here = jnp.concatenate([cache_kv[0], plane_kv[0]], axis=0)
    v_here = jnp.concatenate([cache_kv[1], plane_kv[1]], axis=0)
    count = k_here.shape[0]
    key_rows = jnp.concatenate(
        [
            grp * cache_here + jnp.arange(cache_here, dtype=jnp.int32),
            CACHE + grp * rows_plane + jnp.arange(rows_plane, dtype=jnp.int32),
        ]
    )
    starts = thread_start // STRIDE
    query_rows = jnp.arange(rows_all, dtype=jnp.int32)
    visible = (key_rows[None, :] >= starts[:, None]) & (key_rows[None, :] <= CACHE + query_rows[:, None])

    q_heads = all_q.reshape(rows_all, cols_here, SH, HD)
    k_heads = k_here.reshape(count, cols_here, SH, HD)
    v_heads = v_here.reshape(count, cols_here, SH, HD)
    scores = (
        jnp.einsum("rchd,mchd->chrm", q_heads, k_heads, preferred_element_type=jnp.float32) * scale
    )
    scores = jnp.where(visible, scores, -jnp.inf)
    top = lax.pmax(jnp.max(scores, axis=-1), "grp")
    expo = jnp.exp(scores - top[..., None])
    total = jnp.sum(expo, axis=-1)
    acc = jnp.einsum(
        "chrm,mchd->rchd", expo.astype(jnp.bfloat16), v_heads, preferred_element_type=jnp.float32
    )
    packed = jnp.concatenate(
        [
            acc.reshape(rows_all, cols_here * width_s),
            jnp.transpose(total, (2, 0, 1)).reshape(rows_all, cols_here * SH),
        ],
        axis=1,
    )
    summed = lax.psum_scatter(packed, "grp", scatter_dimension=0, tiled=True)
    acc_mine = summed[:, : cols_here * width_s].reshape(rows_plane, cols_here, SH, HD)
    total_mine = summed[:, cols_here * width_s :].reshape(rows_plane, cols_here, SH)
    mixed = (acc_mine / total_mine[..., None]).astype(jnp.bfloat16)
    mixed = mixed.reshape(rows_plane, cols_here, width_s)
    back = lax.all_to_all(mixed, "seq", split_axis=0, concat_axis=1, tiled=True)
    return back.reshape(tok, width_s)


def shards(queries, keys, values, cache_kv, thread_start):
    width_l = LH * HD
    strided_out = strided_attention(queries, keys, values, cache_kv, thread_start)
    local_out = local_attention(queries[:, :width_l], keys[:, :width_l], values[:, :width_l])
    return jnp.concatenate([local_out.astype(jnp.bfloat16), strided_out], axis=1)


def solution(mesh):
    placed = (
        P(("grp", "seq"), None),
        P(("grp", "seq"), None),
        P(("grp", "seq"), None),
        P(None, "grp", "seq", None),
        P(),
    )
    return jax.shard_map(
        shards, mesh=mesh, in_specs=placed, out_specs=P(("grp", "seq"), None), check_vma=False
    )
```

```python
import jax
import jax.numpy as jnp
from jax import lax
from jax.sharding import PartitionSpec as P

LH = 8
SH = 8
HD = 64
STRIDE = 1024
CACHE = 128


def local_attention(q_part, k_part, v_part):
    scale = HD ** (-0.5)
    tok = q_part.shape[0]
    rows_dev = tok // STRIDE
    block = min(512, STRIDE)
    per_row = STRIDE // block
    q_blocks = q_part.reshape(tok // block, block, LH, HD)
    k_rows = k_part.reshape(rows_dev, STRIDE, LH, HD)
    v_rows = v_part.reshape(rows_dev, STRIDE, LH, HD)
    key_place = jnp.arange(STRIDE, dtype=jnp.int32)

    def one_block(index):
        row_index = index // per_row
        first = index % per_row * block
        query = lax.dynamic_index_in_dim(q_blocks, index, 0, keepdims=False)
        key_row = lax.dynamic_index_in_dim(k_rows, row_index, 0, keepdims=False)
        value_row = lax.dynamic_index_in_dim(v_rows, row_index, 0, keepdims=False)
        scores = (
            jnp.einsum("qhd,khd->hqk", query, key_row, preferred_element_type=jnp.float32) * scale
        )
        causal = (first + jnp.arange(block, dtype=jnp.int32))[:, None] >= key_place[None, :]
        scores = jnp.where(causal[None], scores, -jnp.inf)
        top = jnp.max(scores, axis=-1, keepdims=True)
        expo = jnp.exp(scores - top)
        total = jnp.sum(expo, axis=-1)
        mixed = jnp.einsum(
            "hqk,khd->qhd", expo.astype(jnp.bfloat16), value_row, preferred_element_type=jnp.float32
        )
        return (mixed / jnp.transpose(total)[:, :, None]).reshape(block, LH * HD)

    result = lax.map(one_block, jnp.arange(tok // block, dtype=jnp.int32))
    return result.reshape(tok, LH * HD)


def strided_attention(own_q, own_k, own_v, cache_kv, thread_start):
    scale = HD ** (-0.5)
    width_s = SH * HD
    rows_dev = own_q.shape[0]
    cache_here = cache_kv.shape[1]
    cols_here = cache_kv.shape[2]
    rows_all = thread_start.shape[0]
    grp = lax.axis_index("grp")

    own_kv = jnp.stack([own_k, own_v])
    plane_q = lax.all_to_all(own_q, "seq", split_axis=1, concat_axis=0, tiled=True)
    plane_kv = lax.all_to_all(own_kv, "seq", split_axis=2, concat_axis=1, tiled=True)
    rows_plane = plane_q.shape[0]
    all_q = lax.all_gather(plane_q, "grp", axis=0, tiled=True)

    k_here = jnp.concatenate([cache_kv[0], plane_kv[0]], axis=0)
    v_here = jnp.concatenate([cache_kv[1], plane_kv[1]], axis=0)
    count = k_here.shape[0]
    key_rows = jnp.concatenate(
        [
            grp * cache_here + jnp.arange(cache_here, dtype=jnp.int32),
            CACHE + grp * rows_plane + jnp.arange(rows_plane, dtype=jnp.int32),
        ]
    )
    starts = thread_start // STRIDE
    query_rows = jnp.arange(rows_all, dtype=jnp.int32)
    visible = (key_rows[None, :] >= starts[:, None]) & (key_rows[None, :] <= CACHE + query_rows[:, None])

    q_heads = all_q.reshape(rows_all, cols_here, SH, HD)
    k_heads = k_here.reshape(count, cols_here, SH, HD)
    v_heads = v_here.reshape(count, cols_here, SH, HD)
    scores = (
        jnp.einsum("rchd,mchd->chrm", q_heads, k_heads, preferred_element_type=jnp.float32) * scale
    )
    scores = jnp.where(visible, scores, -jnp.inf)
    top = lax.pmax(jnp.max(scores, axis=-1), "grp")
    expo = jnp.exp(scores - top[..., None])
    total = jnp.sum(expo, axis=-1)
    acc = jnp.einsum(
        "chrm,mchd->rchd", expo.astype(jnp.bfloat16), v_heads, preferred_element_type=jnp.float32
    )
    packed = jnp.concatenate(
        [
            acc.reshape(rows_all, cols_here * width_s),
            jnp.transpose(total, (2, 0, 1)).reshape(rows_all, cols_here * SH),
        ],
        axis=1,
    )
    summed = lax.psum_scatter(packed, "grp", scatter_dimension=0, tiled=True)
    acc_mine = summed[:, : cols_here * width_s].reshape(rows_plane, cols_here, SH, HD)
    total_mine = summed[:, cols_here * width_s :].reshape(rows_plane, cols_here, SH)
    mixed = (acc_mine / total_mine[..., None]).astype(jnp.bfloat16)
    mixed = mixed.reshape(rows_plane, cols_here, width_s)
    return lax.all_to_all(mixed, "seq", split_axis=0, concat_axis=1, tiled=True)


CHUNKS = 2


def shards(queries, keys, values, cache_kv, thread_start):
    width_l = LH * HD
    width_s = SH * HD
    cols_here = cache_kv.shape[2]
    chunks = CHUNKS if cols_here % (CHUNKS * 16) == 0 else 1
    step = cols_here // chunks
    cols_dev = STRIDE // cols_here
    q_cols = queries[:, width_l:].reshape(-1, cols_dev, cols_here, width_s)
    k_cols = keys[:, width_l:].reshape(-1, cols_dev, cols_here, width_s)
    v_cols = values[:, width_l:].reshape(-1, cols_dev, cols_here, width_s)
    pieces = []
    for part in range(chunks):
        cut = slice(part * step, (part + 1) * step)
        pieces.append(
            strided_attention(
                q_cols[:, :, cut].reshape(-1, cols_dev * step, width_s),
                k_cols[:, :, cut].reshape(-1, cols_dev * step, width_s),
                v_cols[:, :, cut].reshape(-1, cols_dev * step, width_s),
                cache_kv[:, :, cut],
                thread_start,
            )
        )
    strided_out = jnp.concatenate(
        [p.reshape(-1, cols_dev, step, width_s) for p in pieces], axis=2
    ).reshape(-1, width_s)
    local_out = local_attention(queries[:, :width_l], keys[:, :width_l], values[:, :width_l])
    return jnp.concatenate([local_out.astype(jnp.bfloat16), strided_out], axis=1)


def solution(mesh):
    placed = (
        P(("grp", "seq"), None),
        P(("grp", "seq"), None),
        P(("grp", "seq"), None),
        P(None, "grp", "seq", None),
        P(),
    )
    return jax.shard_map(
        shards, mesh=mesh, in_specs=placed, out_specs=P(("grp", "seq"), None), check_vma=False
    )
```

```python
import jax
import jax.numpy as jnp
from jax import lax
from jax.sharding import PartitionSpec as P

LH = 8
SH = 8
HD = 64
STRIDE = 1024
CACHE = 128


def local_attention(q_part, k_part, v_part):
    scale = HD ** (-0.5)
    tok = q_part.shape[0]
    rows_dev = tok // STRIDE
    block = min(512, STRIDE)
    per_row = STRIDE // block
    q_blocks = q_part.reshape(tok // block, block, LH, HD)
    k_rows = k_part.reshape(rows_dev, STRIDE, LH, HD)
    v_rows = v_part.reshape(rows_dev, STRIDE, LH, HD)
    key_place = jnp.arange(STRIDE, dtype=jnp.int32)

    def one_block(index):
        row_index = index // per_row
        first = index % per_row * block
        query = lax.dynamic_index_in_dim(q_blocks, index, 0, keepdims=False)
        key_row = lax.dynamic_index_in_dim(k_rows, row_index, 0, keepdims=False)
        value_row = lax.dynamic_index_in_dim(v_rows, row_index, 0, keepdims=False)
        scores = (
            jnp.einsum("qhd,khd->hqk", query, key_row, preferred_element_type=jnp.float32) * scale
        )
        causal = (first + jnp.arange(block, dtype=jnp.int32))[:, None] >= key_place[None, :]
        scores = jnp.where(causal[None], scores, -jnp.inf)
        top = jnp.max(scores, axis=-1, keepdims=True)
        expo = jnp.exp(scores - top)
        total = jnp.sum(expo, axis=-1)
        mixed = jnp.einsum(
            "hqk,khd->qhd", expo.astype(jnp.bfloat16), value_row, preferred_element_type=jnp.float32
        )
        return (mixed / jnp.transpose(total)[:, :, None]).reshape(block, LH * HD)

    result = lax.map(one_block, jnp.arange(tok // block, dtype=jnp.int32))
    return result.reshape(tok, LH * HD)


def group_max(part):
    groups = lax.psum(1, "grp")
    copies = jnp.broadcast_to(part[None], (groups,) + part.shape)
    gathered = lax.all_to_all(copies, "grp", split_axis=0, concat_axis=0, tiled=True)
    return jnp.max(gathered, axis=0)


def strided_attention(own_q, own_k, own_v, cache_kv, thread_start):
    scale = HD ** (-0.5)
    width_s = SH * HD
    rows_dev = own_q.shape[0]
    cache_here = cache_kv.shape[1]
    cols_here = cache_kv.shape[2]
    rows_all = thread_start.shape[0]
    grp = lax.axis_index("grp")

    own_kv = jnp.stack([own_k, own_v])
    plane_q = lax.all_to_all(own_q, "seq", split_axis=1, concat_axis=0, tiled=True)
    plane_kv = lax.all_to_all(own_kv, "seq", split_axis=2, concat_axis=1, tiled=True)
    rows_plane = plane_q.shape[0]
    all_q = lax.all_gather(plane_q, "grp", axis=0, tiled=True)

    k_here = jnp.concatenate([cache_kv[0], plane_kv[0]], axis=0)
    v_here = jnp.concatenate([cache_kv[1], plane_kv[1]], axis=0)
    count = k_here.shape[0]
    key_rows = jnp.concatenate(
        [
            grp * cache_here + jnp.arange(cache_here, dtype=jnp.int32),
            CACHE + grp * rows_plane + jnp.arange(rows_plane, dtype=jnp.int32),
        ]
    )
    starts = thread_start // STRIDE
    query_rows = jnp.arange(rows_all, dtype=jnp.int32)
    visible = (key_rows[None, :] >= starts[:, None]) & (key_rows[None, :] <= CACHE + query_rows[:, None])

    q_heads = all_q.reshape(rows_all, cols_here, SH, HD)
    k_heads = k_here.reshape(count, cols_here, SH, HD)
    v_heads = v_here.reshape(count, cols_here, SH, HD)
    scores = (
        jnp.einsum("rchd,mchd->chrm", q_heads, k_heads, preferred_element_type=jnp.float32) * scale
    )
    scores = jnp.where(visible, scores, -jnp.inf)
    top = group_max(jnp.max(scores, axis=-1))
    expo = jnp.exp(scores - top[..., None])
    total = jnp.sum(expo, axis=-1)
    acc = jnp.einsum(
        "chrm,mchd->rchd", expo.astype(jnp.bfloat16), v_heads, preferred_element_type=jnp.float32
    )
    packed = jnp.concatenate(
        [
            acc.reshape(rows_all, cols_here * width_s),
            jnp.transpose(total, (2, 0, 1)).reshape(rows_all, cols_here * SH),
        ],
        axis=1,
    )
    return packed, rows_plane


def strided_finish(packed, rows_plane):
    width_s = SH * HD
    cols_here = (packed.shape[1]) // (width_s + SH)
    summed = lax.psum_scatter(packed, "grp", scatter_dimension=0, tiled=True)
    acc_mine = summed[:, : cols_here * width_s].reshape(rows_plane, cols_here, SH, HD)
    total_mine = summed[:, cols_here * width_s :].reshape(rows_plane, cols_here, SH)
    mixed = (acc_mine / total_mine[..., None]).astype(jnp.bfloat16)
    mixed = mixed.reshape(rows_plane, cols_here, width_s)
    return lax.all_to_all(mixed, "seq", split_axis=0, concat_axis=1, tiled=True)


CHUNKS = 2


def shards(queries, keys, values, cache_kv, thread_start):
    width_l = LH * HD
    width_s = SH * HD
    cols_here = cache_kv.shape[2]
    chunks = CHUNKS if cols_here % (CHUNKS * 16) == 0 else 1
    step = cols_here // chunks
    cols_dev = STRIDE // cols_here
    q_cols = queries[:, width_l:].reshape(-1, cols_dev, cols_here, width_s)
    k_cols = keys[:, width_l:].reshape(-1, cols_dev, cols_here, width_s)
    v_cols = values[:, width_l:].reshape(-1, cols_dev, cols_here, width_s)
    partials = []
    for part in range(chunks):
        cut = slice(part * step, (part + 1) * step)
        partials.append(
            strided_attention(
                q_cols[:, :, cut].reshape(-1, cols_dev * step, width_s),
                k_cols[:, :, cut].reshape(-1, cols_dev * step, width_s),
                v_cols[:, :, cut].reshape(-1, cols_dev * step, width_s),
                cache_kv[:, :, cut],
                thread_start,
            )
        )
    local_out = local_attention(queries[:, :width_l], keys[:, :width_l], values[:, :width_l])
    last, local_out = lax.optimization_barrier((partials[-1][0], local_out))
    partials[-1] = (last, partials[-1][1])
    pieces = [strided_finish(*p) for p in partials]
    strided_out = jnp.concatenate(
        [p.reshape(-1, cols_dev, step, width_s) for p in pieces], axis=2
    ).reshape(-1, width_s)
    return jnp.concatenate([local_out.astype(jnp.bfloat16), strided_out], axis=1)


def solution(mesh):
    placed = (
        P(("grp", "seq"), None),
        P(("grp", "seq"), None),
        P(("grp", "seq"), None),
        P(None, "grp", "seq", None),
        P(),
    )
    return jax.shard_map(
        shards, mesh=mesh, in_specs=placed, out_specs=P(("grp", "seq"), None), check_vma=False
    )
```

```python
import jax
import jax.numpy as jnp
from jax import lax
from jax.sharding import PartitionSpec as P

LH = 8
SH = 8
HD = 64
STRIDE = 1024
CACHE = 128


def local_attention(q_part, k_part, v_part):
    scale = HD ** (-0.5)
    tok = q_part.shape[0]
    rows_dev = tok // STRIDE
    block = min(512, STRIDE)
    per_row = STRIDE // block
    q_blocks = q_part.reshape(tok // block, block, LH, HD)
    k_rows = k_part.reshape(rows_dev, STRIDE, LH, HD)
    v_rows = v_part.reshape(rows_dev, STRIDE, LH, HD)
    key_place = jnp.arange(STRIDE, dtype=jnp.int32)

    def one_block(index):
        row_index = index // per_row
        first = index % per_row * block
        query = lax.dynamic_index_in_dim(q_blocks, index, 0, keepdims=False)
        key_row = lax.dynamic_index_in_dim(k_rows, row_index, 0, keepdims=False)
        value_row = lax.dynamic_index_in_dim(v_rows, row_index, 0, keepdims=False)
        scores = (
            jnp.einsum("qhd,khd->hqk", query, key_row, preferred_element_type=jnp.float32) * scale
        )
        causal = (first + jnp.arange(block, dtype=jnp.int32))[:, None] >= key_place[None, :]
        scores = jnp.where(causal[None], scores, -jnp.inf)
        top = jnp.max(scores, axis=-1, keepdims=True)
        expo = jnp.exp(scores - top)
        total = jnp.sum(expo, axis=-1)
        mixed = jnp.einsum(
            "hqk,khd->qhd", expo.astype(jnp.bfloat16), value_row, preferred_element_type=jnp.float32
        )
        return (mixed / jnp.transpose(total)[:, :, None]).reshape(block, LH * HD)

    result = lax.map(one_block, jnp.arange(tok // block, dtype=jnp.int32))
    return result.reshape(tok, LH * HD)


def group_max(part):
    groups = lax.psum(1, "grp")
    copies = jnp.broadcast_to(part[None], (groups,) + part.shape)
    gathered = lax.all_to_all(copies, "grp", split_axis=0, concat_axis=0, tiled=True)
    return jnp.max(gathered, axis=0)


def strided_attention(own_q, own_k, own_v, cache_kv, thread_start):
    scale = HD ** (-0.5)
    width_s = SH * HD
    rows_dev = own_q.shape[0]
    cache_here = cache_kv.shape[1]
    cols_here = cache_kv.shape[2]
    rows_all = thread_start.shape[0]
    grp = lax.axis_index("grp")

    own_kv = jnp.stack([own_k, own_v])
    plane_q = lax.all_to_all(own_q, "seq", split_axis=1, concat_axis=0, tiled=True)
    plane_kv = lax.all_to_all(own_kv, "seq", split_axis=2, concat_axis=1, tiled=True)
    return plane_q, plane_kv, cache_kv


def strided_partials(all_q, plane_kv, cache_kv, thread_start):
    scale = HD ** (-0.5)
    width_s = SH * HD
    cache_here = cache_kv.shape[1]
    cols_here = cache_kv.shape[2]
    rows_all = thread_start.shape[0]
    rows_plane = plane_kv.shape[1]
    grp = lax.axis_index("grp")

    k_here = jnp.concatenate([cache_kv[0], plane_kv[0]], axis=0)
    v_here = jnp.concatenate([cache_kv[1], plane_kv[1]], axis=0)
    count = k_here.shape[0]
    key_rows = jnp.concatenate(
        [
            grp * cache_here + jnp.arange(cache_here, dtype=jnp.int32),
            CACHE + grp * rows_plane + jnp.arange(rows_plane, dtype=jnp.int32),
        ]
    )
    starts = thread_start // STRIDE
    query_rows = jnp.arange(rows_all, dtype=jnp.int32)
    visible = (key_rows[None, :] >= starts[:, None]) & (key_rows[None, :] <= CACHE + query_rows[:, None])

    q_heads = all_q.reshape(rows_all, cols_here, SH, HD)
    k_heads = k_here.reshape(count, cols_here, SH, HD)
    v_heads = v_here.reshape(count, cols_here, SH, HD)
    scores = (
        jnp.einsum("rchd,mchd->chrm", q_heads, k_heads, preferred_element_type=jnp.float32) * scale
    )
    scores = jnp.where(visible, scores, -jnp.inf)
    top = group_max(jnp.max(scores, axis=-1))
    expo = jnp.exp(scores - top[..., None])
    total = jnp.sum(expo, axis=-1)
    acc = jnp.einsum(
        "chrm,mchd->rchd", expo.astype(jnp.bfloat16), v_heads, preferred_element_type=jnp.float32
    )
    packed = jnp.concatenate(
        [
            acc.reshape(rows_all, cols_here * width_s),
            jnp.transpose(total, (2, 0, 1)).reshape(rows_all, cols_here * SH),
        ],
        axis=1,
    )
    return packed, rows_plane


def strided_finish(packed, rows_plane):
    width_s = SH * HD
    cols_here = (packed.shape[1]) // (width_s + SH)
    summed = lax.psum_scatter(packed, "grp", scatter_dimension=0, tiled=True)
    acc_mine = summed[:, : cols_here * width_s].reshape(rows_plane, cols_here, SH, HD)
    total_mine = summed[:, cols_here * width_s :].reshape(rows_plane, cols_here, SH)
    mixed = (acc_mine / total_mine[..., None]).astype(jnp.bfloat16)
    mixed = mixed.reshape(rows_plane, cols_here, width_s)
    return lax.all_to_all(mixed, "seq", split_axis=0, concat_axis=1, tiled=True)


CHUNKS = 2


def shards(queries, keys, values, cache_kv, thread_start):
    width_l = LH * HD
    width_s = SH * HD
    cols_here = cache_kv.shape[2]
    chunks = CHUNKS if cols_here % (CHUNKS * 16) == 0 else 1
    step = cols_here // chunks
    cols_dev = STRIDE // cols_here
    q_cols = queries[:, width_l:].reshape(-1, cols_dev, cols_here, width_s)
    k_cols = keys[:, width_l:].reshape(-1, cols_dev, cols_here, width_s)
    v_cols = values[:, width_l:].reshape(-1, cols_dev, cols_here, width_s)
    gathered = []
    for part in range(chunks):
        cut = slice(part * step, (part + 1) * step)
        gathered.append(
            strided_attention(
                q_cols[:, :, cut].reshape(-1, cols_dev * step, width_s),
                k_cols[:, :, cut].reshape(-1, cols_dev * step, width_s),
                v_cols[:, :, cut].reshape(-1, cols_dev * step, width_s),
                cache_kv[:, :, cut],
                thread_start,
            )
        )
    planes = tuple(g[0] for g in gathered)
    gathered = [[lax.all_gather(g[0], "grp", axis=0, tiled=True), g[1], g[2]] for g in gathered]
    gathered[0][0], planes = lax.optimization_barrier((gathered[0][0], planes))
    pieces = []
    local_in = (queries[:, :width_l], keys[:, :width_l], values[:, :width_l])
    local_out = None
    for part in range(chunks):
        packed, rows_plane = strided_partials(*gathered[part], thread_start)
        pieces.append(strided_finish(packed, rows_plane))
        if part == 0:
            packed, local_in = lax.optimization_barrier((packed, local_in))
            local_out = local_attention(*local_in)
            if chunks > 1:
                local_out, gathered[1] = lax.optimization_barrier((local_out, gathered[1]))
        elif part + 1 < chunks:
            packed, gathered[part + 1] = lax.optimization_barrier((packed, gathered[part + 1]))
    strided_out = jnp.concatenate(
        [p.reshape(-1, cols_dev, step, width_s) for p in pieces], axis=2
    ).reshape(-1, width_s)
    return jnp.concatenate([local_out.astype(jnp.bfloat16), strided_out], axis=1)


def solution(mesh):
    placed = (
        P(("grp", "seq"), None),
        P(("grp", "seq"), None),
        P(("grp", "seq"), None),
        P(None, "grp", "seq", None),
        P(),
    )
    return jax.shard_map(
        shards, mesh=mesh, in_specs=placed, out_specs=P(("grp", "seq"), None), check_vma=False
    )
```

```python
import jax
import jax.numpy as jnp
from jax import lax
from jax.experimental import pallas as pl
from jax.sharding import PartitionSpec as P

LH = 8
SH = 8
HD = 64
STRIDE = 1024
CACHE = 128


def local_attention(q_part, k_part, v_part):
    scale = HD ** (-0.5)
    tok = q_part.shape[0]
    rows_dev = tok // STRIDE
    block = min(512, STRIDE)
    per_row = STRIDE // block
    q_blocks = q_part.reshape(tok // block, block, LH, HD)
    k_rows = k_part.reshape(rows_dev, STRIDE, LH, HD)
    v_rows = v_part.reshape(rows_dev, STRIDE, LH, HD)
    key_place = jnp.arange(STRIDE, dtype=jnp.int32)

    def one_block(index):
        row_index = index // per_row
        first = index % per_row * block
        query = lax.dynamic_index_in_dim(q_blocks, index, 0, keepdims=False)
        key_row = lax.dynamic_index_in_dim(k_rows, row_index, 0, keepdims=False)
        value_row = lax.dynamic_index_in_dim(v_rows, row_index, 0, keepdims=False)
        scores = (
            jnp.einsum("qhd,khd->hqk", query, key_row, preferred_element_type=jnp.float32) * scale
        )
        causal = (first + jnp.arange(block, dtype=jnp.int32))[:, None] >= key_place[None, :]
        scores = jnp.where(causal[None], scores, -jnp.inf)
        top = jnp.max(scores, axis=-1, keepdims=True)
        expo = jnp.exp(scores - top)
        total = jnp.sum(expo, axis=-1)
        mixed = jnp.einsum(
            "hqk,khd->qhd", expo.astype(jnp.bfloat16), value_row, preferred_element_type=jnp.float32
        )
        return (mixed / jnp.transpose(total)[:, :, None]).reshape(block, LH * HD)

    result = lax.map(one_block, jnp.arange(tok // block, dtype=jnp.int32))
    return result.reshape(tok, LH * HD)


def group_max(part):
    groups = lax.psum(1, "grp")
    copies = jnp.broadcast_to(part[None], (groups,) + part.shape)
    gathered = lax.all_to_all(copies, "grp", split_axis=0, concat_axis=0, tiled=True)
    return jnp.max(gathered, axis=0)


def strided_attention(own_q, own_k, own_v, cache_kv, thread_start):
    scale = HD ** (-0.5)
    width_s = SH * HD
    rows_dev = own_q.shape[0]
    cache_here = cache_kv.shape[1]
    cols_here = cache_kv.shape[2]
    rows_all = thread_start.shape[0]
    grp = lax.axis_index("grp")

    own_kv = jnp.stack([own_k, own_v])
    plane_q = lax.all_to_all(own_q, "seq", split_axis=1, concat_axis=0, tiled=True)
    plane_kv = lax.all_to_all(own_kv, "seq", split_axis=2, concat_axis=1, tiled=True)
    return plane_q, plane_kv


BLOCK = 8


def _bias(key_rows, starts, rows_all):
    count = key_rows.shape[0]
    place = jnp.arange(rows_all * BLOCK, dtype=jnp.int32)
    spot = jnp.arange(count * BLOCK, dtype=jnp.int32)
    row = place // BLOCK
    key = key_rows[spot // BLOCK]
    seen = (
        (key[None, :] >= starts[row][:, None])
        & (key[None, :] <= CACHE + row[:, None])
        & ((place % BLOCK)[:, None] == (spot % BLOCK)[None, :])
    )
    return jnp.where(seen, 0.0, -jnp.inf).astype(jnp.float32)


def _head(ref, h):
    part = ref[:, :, h * HD : (h + 1) * HD].astype(jnp.float32)
    return part.reshape(part.shape[0] * BLOCK, HD).astype(jnp.bfloat16)


def _scores(q_ref, kc_ref, kw_ref, bc_ref, bw_ref, h):
    scale = HD ** (-0.5)
    q = _head(q_ref, h)
    dims = (((1,), (1,)), ((), ()))
    sc = lax.dot_general(q, _head(kc_ref, h), dims, preferred_element_type=jnp.float32)
    sw = lax.dot_general(q, _head(kw_ref, h), dims, preferred_element_type=jnp.float32)
    return sc * scale + bc_ref[...], sw * scale + bw_ref[...]


def _max_kernel(q_ref, kc_ref, kw_ref, bc_ref, bw_ref, top_ref):
    for h in range(SH):
        sc, sw = _scores(q_ref, kc_ref, kw_ref, bc_ref, bw_ref, h)
        top_ref[:, h : h + 1] = jnp.maximum(
            jnp.max(sc, axis=1, keepdims=True), jnp.max(sw, axis=1, keepdims=True)
        )


def _sum_kernel(q_ref, kc_ref, kw_ref, vc_ref, vw_ref, bc_ref, bw_ref, top_ref, acc_ref, tot_ref):
    rows = q_ref.shape[0]
    for h in range(SH):
        sc, sw = _scores(q_ref, kc_ref, kw_ref, bc_ref, bw_ref, h)
        top = top_ref[:, h : h + 1]
        ec = jnp.exp(sc - top)
        ew = jnp.exp(sw - top)
        tot = jnp.sum(ec, axis=1, keepdims=True) + jnp.sum(ew, axis=1, keepdims=True)
        acc = jnp.dot(
            ec.astype(jnp.bfloat16), _head(vc_ref, h), preferred_element_type=jnp.float32
        ) + jnp.dot(ew.astype(jnp.bfloat16), _head(vw_ref, h), preferred_element_type=jnp.float32)
        acc_ref[:, :, h * HD : (h + 1) * HD] = acc.reshape(rows, BLOCK, HD)
        tot_ref[:, :, h : h + 1] = tot.reshape(rows, BLOCK, 1)


def strided_partials(all_q, plane_kv, cache_kv, offset, thread_start):
    width_s = SH * HD
    rows_all, cols_chunk, _ = all_q.shape
    cache_here = cache_kv.shape[1]
    rows_plane = plane_kv.shape[1]
    grp = lax.axis_index("grp")
    starts = thread_start // STRIDE
    bias_c = _bias(grp * cache_here + jnp.arange(cache_here, dtype=jnp.int32), starts, rows_all)
    bias_w = _bias(
        CACHE + grp * rows_plane + jnp.arange(rows_plane, dtype=jnp.int32), starts, rows_all
    )
    blocks = cols_chunk // BLOCK
    first = offset // BLOCK
    q_spec = pl.BlockSpec((rows_all, BLOCK, width_s), lambda j: (0, j, 0))
    kc_spec = pl.BlockSpec((None, cache_here, BLOCK, width_s), lambda j: (0, 0, first + j, 0))
    vc_spec = pl.BlockSpec((None, cache_here, BLOCK, width_s), lambda j: (1, 0, first + j, 0))
    kw_spec = pl.BlockSpec((None, rows_plane, BLOCK, width_s), lambda j: (0, 0, j, 0))
    vw_spec = pl.BlockSpec((None, rows_plane, BLOCK, width_s), lambda j: (1, 0, j, 0))
    bc_spec = pl.BlockSpec(bias_c.shape, lambda j: (0, 0))
    bw_spec = pl.BlockSpec(bias_w.shape, lambda j: (0, 0))
    top_spec = pl.BlockSpec((None, rows_all * BLOCK, SH), lambda j: (j, 0, 0))
    top_shape = jax.ShapeDtypeStruct((blocks, rows_all * BLOCK, SH), jnp.float32)
    top_part = pl.pallas_call(
        _max_kernel,
        grid=(blocks,),
        in_specs=[q_spec, kc_spec, kw_spec, bc_spec, bw_spec],
        out_specs=top_spec,
        out_shape=top_shape,
    )(all_q, cache_kv, plane_kv, bias_c, bias_w)
    top = group_max(top_part.reshape(-1, 128)).reshape(top_shape.shape)
    acc, tot = pl.pallas_call(
        _sum_kernel,
        grid=(blocks,),
        in_specs=[q_spec, kc_spec, kw_spec, vc_spec, vw_spec, bc_spec, bw_spec, top_spec],
        out_specs=[
            pl.BlockSpec((rows_all, BLOCK, width_s), lambda j: (0, j, 0)),
            pl.BlockSpec((rows_all, BLOCK, SH), lambda j: (0, j, 0)),
        ],
        out_shape=[
            jax.ShapeDtypeStruct((rows_all, cols_chunk, width_s), jnp.float32),
            jax.ShapeDtypeStruct((rows_all, cols_chunk, SH), jnp.float32),
        ],
    )(all_q, cache_kv, plane_kv, cache_kv, plane_kv, bias_c, bias_w, top)
    packed = jnp.concatenate(
        [acc.reshape(rows_all, cols_chunk * width_s), tot.reshape(rows_all, cols_chunk * SH)],
        axis=1,
    )
    return packed, rows_plane


def strided_finish(packed, rows_plane):
    width_s = SH * HD
    cols_here = (packed.shape[1]) // (width_s + SH)
    summed = lax.psum_scatter(packed, "grp", scatter_dimension=0, tiled=True)
    acc_mine = summed[:, : cols_here * width_s].reshape(rows_plane, cols_here, SH, HD)
    total_mine = summed[:, cols_here * width_s :].reshape(rows_plane, cols_here, SH)
    mixed = (acc_mine / total_mine[..., None]).astype(jnp.bfloat16)
    mixed = mixed.reshape(rows_plane, cols_here, width_s)
    return lax.all_to_all(mixed, "seq", split_axis=0, concat_axis=1, tiled=True)


CHUNKS = 2


def shards(queries, keys, values, cache_kv, thread_start):
    width_l = LH * HD
    width_s = SH * HD
    cols_here = cache_kv.shape[2]
    chunks = CHUNKS if cols_here % (CHUNKS * 16) == 0 else 1
    step = cols_here // chunks
    cols_dev = STRIDE // cols_here
    q_cols = queries[:, width_l:].reshape(-1, cols_dev, cols_here, width_s)
    k_cols = keys[:, width_l:].reshape(-1, cols_dev, cols_here, width_s)
    v_cols = values[:, width_l:].reshape(-1, cols_dev, cols_here, width_s)
    gathered = []
    for part in range(chunks):
        cut = slice(part * step, (part + 1) * step)
        gathered.append(
            strided_attention(
                q_cols[:, :, cut].reshape(-1, cols_dev * step, width_s),
                k_cols[:, :, cut].reshape(-1, cols_dev * step, width_s),
                v_cols[:, :, cut].reshape(-1, cols_dev * step, width_s),
                cache_kv,
                thread_start,
            )
        )
    planes = tuple(g[0] for g in gathered)
    gathered = [[lax.all_gather(g[0], "grp", axis=0, tiled=True), g[1]] for g in gathered]
    gathered[0][0], planes = lax.optimization_barrier((gathered[0][0], planes))
    pieces = []
    local_in = (queries[:, :width_l], keys[:, :width_l], values[:, :width_l])
    local_out = None
    for part in range(chunks):
        packed, rows_plane = strided_partials(*gathered[part], cache_kv, part * step, thread_start)
        pieces.append(strided_finish(packed, rows_plane))
        if part == 0:
            packed, local_in = lax.optimization_barrier((packed, local_in))
            local_out = local_attention(*local_in)
            if chunks > 1:
                local_out, gathered[1] = lax.optimization_barrier((local_out, gathered[1]))
        elif part + 1 < chunks:
            packed, gathered[part + 1] = lax.optimization_barrier((packed, gathered[part + 1]))
    strided_out = jnp.concatenate(
        [p.reshape(-1, cols_dev, step, width_s) for p in pieces], axis=2
    ).reshape(-1, width_s)
    return jnp.concatenate([local_out.astype(jnp.bfloat16), strided_out], axis=1)


def solution(mesh):
    placed = (
        P(("grp", "seq"), None),
        P(("grp", "seq"), None),
        P(("grp", "seq"), None),
        P(None, "grp", "seq", None),
        P(),
    )
    return jax.shard_map(
        shards, mesh=mesh, in_specs=placed, out_specs=P(("grp", "seq"), None), check_vma=False
    )
```

```python
import jax
import jax.numpy as jnp
from jax import lax
from jax.experimental import pallas as pl
from jax.sharding import PartitionSpec as P

LH = 8
SH = 8
HD = 64
STRIDE = 1024
CACHE = 128


def local_attention(q_part, k_part, v_part):
    scale = HD ** (-0.5)
    tok = q_part.shape[0]
    rows_dev = tok // STRIDE
    block = min(512, STRIDE)
    per_row = STRIDE // block
    q_blocks = q_part.reshape(tok // block, block, LH, HD)
    k_rows = k_part.reshape(rows_dev, STRIDE, LH, HD)
    v_rows = v_part.reshape(rows_dev, STRIDE, LH, HD)
    key_place = jnp.arange(STRIDE, dtype=jnp.int32)

    def one_block(index):
        row_index = index // per_row
        first = index % per_row * block
        query = lax.dynamic_index_in_dim(q_blocks, index, 0, keepdims=False)
        key_row = lax.dynamic_index_in_dim(k_rows, row_index, 0, keepdims=False)
        value_row = lax.dynamic_index_in_dim(v_rows, row_index, 0, keepdims=False)
        scores = (
            jnp.einsum("qhd,khd->hqk", query, key_row, preferred_element_type=jnp.float32) * scale
        )
        causal = (first + jnp.arange(block, dtype=jnp.int32))[:, None] >= key_place[None, :]
        scores = jnp.where(causal[None], scores, -jnp.inf)
        top = jnp.max(scores, axis=-1, keepdims=True)
        expo = jnp.exp(scores - top)
        total = jnp.sum(expo, axis=-1)
        mixed = jnp.einsum(
            "hqk,khd->qhd", expo.astype(jnp.bfloat16), value_row, preferred_element_type=jnp.float32
        )
        return (mixed / jnp.transpose(total)[:, :, None]).reshape(block, LH * HD)

    result = [one_block(index) for index in range(tok // block)]
    return jnp.concatenate(result, axis=0)


def group_max(part):
    groups = lax.psum(1, "grp")
    copies = jnp.broadcast_to(part[None], (groups,) + part.shape)
    gathered = lax.all_to_all(copies, "grp", split_axis=0, concat_axis=0, tiled=True)
    return jnp.max(gathered, axis=0)


def strided_attention(own_q, own_k, own_v, cache_kv, thread_start):
    scale = HD ** (-0.5)
    width_s = SH * HD
    rows_dev = own_q.shape[0]
    cache_here = cache_kv.shape[1]
    cols_here = cache_kv.shape[2]
    rows_all = thread_start.shape[0]
    grp = lax.axis_index("grp")

    own_kv = jnp.stack([own_k, own_v])
    plane_q = lax.all_to_all(own_q, "seq", split_axis=1, concat_axis=0, tiled=True)
    plane_kv = lax.all_to_all(own_kv, "seq", split_axis=2, concat_axis=1, tiled=True)
    return plane_q, plane_kv


BLOCK = 8


def _bias(first_key, count, starts, rows_all):
    shape = (rows_all * BLOCK, count * BLOCK)
    place = lax.broadcasted_iota(jnp.int32, shape, 0)
    spot = lax.broadcasted_iota(jnp.int32, shape, 1)
    row = place // BLOCK
    key = first_key + spot // BLOCK
    start = jnp.broadcast_to(starts[:, None], (rows_all, BLOCK)).reshape(rows_all * BLOCK, 1)
    seen = (key >= start) & (key <= CACHE + row) & (place % BLOCK == spot % BLOCK)
    return jnp.where(seen, 0.0, -jnp.inf).astype(jnp.float32)


def _head(ref, h):
    part = ref[:, :, h * HD : (h + 1) * HD].astype(jnp.float32)
    return part.reshape(part.shape[0] * BLOCK, HD).astype(jnp.bfloat16)


def _scores(q_ref, kc_ref, kw_ref, bc_ref, bw_ref, h):
    scale = HD ** (-0.5)
    q = _head(q_ref, h)
    dims = (((1,), (1,)), ((), ()))
    sc = lax.dot_general(q, _head(kc_ref, h), dims, preferred_element_type=jnp.float32)
    sw = lax.dot_general(q, _head(kw_ref, h), dims, preferred_element_type=jnp.float32)
    return sc * scale + bc_ref[...], sw * scale + bw_ref[...]


def _max_kernel(q_ref, kc_ref, kw_ref, bc_ref, bw_ref, top_ref):
    for h in range(SH):
        sc, sw = _scores(q_ref, kc_ref, kw_ref, bc_ref, bw_ref, h)
        top_ref[:, h : h + 1] = jnp.maximum(
            jnp.max(sc, axis=1, keepdims=True), jnp.max(sw, axis=1, keepdims=True)
        )


def _sum_kernel(q_ref, kc_ref, kw_ref, vc_ref, vw_ref, bc_ref, bw_ref, top_ref, acc_ref, tot_ref):
    rows = q_ref.shape[0]
    for h in range(SH):
        sc, sw = _scores(q_ref, kc_ref, kw_ref, bc_ref, bw_ref, h)
        top = top_ref[:, h : h + 1]
        ec = jnp.exp(sc - top)
        ew = jnp.exp(sw - top)
        tot = jnp.sum(ec, axis=1, keepdims=True) + jnp.sum(ew, axis=1, keepdims=True)
        acc = jnp.dot(
            ec.astype(jnp.bfloat16), _head(vc_ref, h), preferred_element_type=jnp.float32
        ) + jnp.dot(ew.astype(jnp.bfloat16), _head(vw_ref, h), preferred_element_type=jnp.float32)
        acc_ref[:, :, h * HD : (h + 1) * HD] = acc.reshape(rows, BLOCK, HD)
        tot_ref[:, :, h : h + 1] = tot.reshape(rows, BLOCK, 1)


def strided_biases(cache_here, rows_plane, thread_start):
    rows_all = thread_start.shape[0]
    grp = lax.axis_index("grp")
    starts = thread_start // STRIDE
    bias_c = _bias(grp * cache_here, cache_here, starts, rows_all)
    bias_w = _bias(CACHE + grp * rows_plane, rows_plane, starts, rows_all)
    return bias_c, bias_w


def strided_partials(all_q, plane_kv, cache_kv, offset, biases):
    width_s = SH * HD
    rows_all, cols_chunk, _ = all_q.shape
    cache_here = cache_kv.shape[1]
    rows_plane = plane_kv.shape[1]
    bias_c, bias_w = biases
    blocks = cols_chunk // BLOCK
    first = offset // BLOCK
    q_spec = pl.BlockSpec((rows_all, BLOCK, width_s), lambda j: (0, j, 0))
    kc_spec = pl.BlockSpec((None, cache_here, BLOCK, width_s), lambda j: (0, 0, first + j, 0))
    vc_spec = pl.BlockSpec((None, cache_here, BLOCK, width_s), lambda j: (1, 0, first + j, 0))
    kw_spec = pl.BlockSpec((None, rows_plane, BLOCK, width_s), lambda j: (0, 0, j, 0))
    vw_spec = pl.BlockSpec((None, rows_plane, BLOCK, width_s), lambda j: (1, 0, j, 0))
    bc_spec = pl.BlockSpec(bias_c.shape, lambda j: (0, 0))
    bw_spec = pl.BlockSpec(bias_w.shape, lambda j: (0, 0))
    top_spec = pl.BlockSpec((None, rows_all * BLOCK, SH), lambda j: (j, 0, 0))
    top_shape = jax.ShapeDtypeStruct((blocks, rows_all * BLOCK, SH), jnp.float32)
    top_part = pl.pallas_call(
        _max_kernel,
        grid=(blocks,),
        in_specs=[q_spec, kc_spec, kw_spec, bc_spec, bw_spec],
        out_specs=top_spec,
        out_shape=top_shape,
    )(all_q, cache_kv, plane_kv, bias_c, bias_w)
    top = group_max(top_part.reshape(-1, 128)).reshape(top_shape.shape)
    acc, tot = pl.pallas_call(
        _sum_kernel,
        grid=(blocks,),
        in_specs=[q_spec, kc_spec, kw_spec, vc_spec, vw_spec, bc_spec, bw_spec, top_spec],
        out_specs=[
            pl.BlockSpec((rows_all, BLOCK, width_s), lambda j: (0, j, 0)),
            pl.BlockSpec((rows_all, BLOCK, SH), lambda j: (0, j, 0)),
        ],
        out_shape=[
            jax.ShapeDtypeStruct((rows_all, cols_chunk, width_s), jnp.float32),
            jax.ShapeDtypeStruct((rows_all, cols_chunk, SH), jnp.float32),
        ],
    )(all_q, cache_kv, plane_kv, cache_kv, plane_kv, bias_c, bias_w, top)
    packed = jnp.concatenate(
        [acc.reshape(rows_all, cols_chunk * width_s), tot.reshape(rows_all, cols_chunk * SH)],
        axis=1,
    )
    return packed, rows_plane


def strided_finish(packed, rows_plane):
    width_s = SH * HD
    cols_here = (packed.shape[1]) // (width_s + SH)
    summed = lax.psum_scatter(packed, "grp", scatter_dimension=0, tiled=True)
    acc_mine = summed[:, : cols_here * width_s].reshape(rows_plane, cols_here, SH, HD)
    total_mine = summed[:, cols_here * width_s :].reshape(rows_plane, cols_here, SH)
    mixed = (acc_mine / total_mine[..., None]).astype(jnp.bfloat16)
    mixed = mixed.reshape(rows_plane, cols_here, width_s)
    return lax.all_to_all(mixed, "seq", split_axis=0, concat_axis=1, tiled=True)


CHUNKS = 2


def shards(queries, keys, values, cache_kv, thread_start):
    width_l = LH * HD
    width_s = SH * HD
    cols_here = cache_kv.shape[2]
    chunks = CHUNKS if cols_here % (CHUNKS * 16) == 0 else 1
    step = cols_here // chunks
    cols_dev = STRIDE // cols_here
    q_cols = queries[:, width_l:].reshape(-1, cols_dev, cols_here, width_s)
    k_cols = keys[:, width_l:].reshape(-1, cols_dev, cols_here, width_s)
    v_cols = values[:, width_l:].reshape(-1, cols_dev, cols_here, width_s)
    gathered = []
    for part in range(chunks):
        cut = slice(part * step, (part + 1) * step)
        gathered.append(
            strided_attention(
                q_cols[:, :, cut].reshape(-1, cols_dev * step, width_s),
                k_cols[:, :, cut].reshape(-1, cols_dev * step, width_s),
                v_cols[:, :, cut].reshape(-1, cols_dev * step, width_s),
                cache_kv,
                thread_start,
            )
        )
    planes = tuple(g[0] for g in gathered)
    gathered = [[lax.all_gather(g[0], "grp", axis=0, tiled=True), g[1]] for g in gathered]
    gathered[0][0], planes = lax.optimization_barrier((gathered[0][0], planes))
    biases = strided_biases(cache_kv.shape[1], gathered[0][1].shape[1], thread_start)
    pieces = []
    local_in = (queries[:, :width_l], keys[:, :width_l], values[:, :width_l])
    for part in range(chunks):
        packed, rows_plane = strided_partials(*gathered[part], cache_kv, part * step, biases)
        if part + 1 < chunks:
            packed, gathered[part + 1] = lax.optimization_barrier((packed, gathered[part + 1]))
        else:
            packed, local_in = lax.optimization_barrier((packed, local_in))
        pieces.append(strided_finish(packed, rows_plane))
    local_out = local_attention(*local_in)
    strided_out = jnp.concatenate(
        [p.reshape(-1, cols_dev, step, width_s) for p in pieces], axis=2
    ).reshape(-1, width_s)
    return jnp.concatenate([local_out.astype(jnp.bfloat16), strided_out], axis=1)


def solution(mesh):
    placed = (
        P(("grp", "seq"), None),
        P(("grp", "seq"), None),
        P(("grp", "seq"), None),
        P(None, "grp", "seq", None),
        P(),
    )
    return jax.shard_map(
        shards, mesh=mesh, in_specs=placed, out_specs=P(("grp", "seq"), None), check_vma=False
    )
```

```python
import jax
import jax.numpy as jnp
from jax import lax
from jax.experimental import pallas as pl
from jax.sharding import PartitionSpec as P

LH = 8
SH = 8
HD = 64
STRIDE = 1024
CACHE = 128


def local_attention(q_part, k_part, v_part):
    scale = HD ** (-0.5)
    tok = q_part.shape[0]
    rows_dev = tok // STRIDE
    block = min(512, STRIDE)
    per_row = STRIDE // block
    q_blocks = q_part.reshape(tok // block, block, LH, HD)
    k_rows = k_part.reshape(rows_dev, STRIDE, LH, HD)
    v_rows = v_part.reshape(rows_dev, STRIDE, LH, HD)
    key_place = jnp.arange(STRIDE, dtype=jnp.int32)

    def one_block(index):
        row_index = index // per_row
        first = index % per_row * block
        query = lax.dynamic_index_in_dim(q_blocks, index, 0, keepdims=False)
        key_row = lax.dynamic_index_in_dim(k_rows, row_index, 0, keepdims=False)
        value_row = lax.dynamic_index_in_dim(v_rows, row_index, 0, keepdims=False)
        scores = (
            jnp.einsum("qhd,khd->hqk", query, key_row, preferred_element_type=jnp.float32) * scale
        )
        causal = (first + jnp.arange(block, dtype=jnp.int32))[:, None] >= key_place[None, :]
        scores = jnp.where(causal[None], scores, -jnp.inf)
        top = jnp.max(scores, axis=-1, keepdims=True)
        expo = jnp.exp(scores - top)
        total = jnp.sum(expo, axis=-1)
        mixed = jnp.einsum(
            "hqk,khd->qhd", expo.astype(jnp.bfloat16), value_row, preferred_element_type=jnp.float32
        )
        return (mixed / jnp.transpose(total)[:, :, None]).reshape(block, LH * HD)

    result = [one_block(index) for index in range(tok // block)]
    return jnp.concatenate(result, axis=0)


def group_max(part):
    groups = lax.psum(1, "grp")
    copies = jnp.broadcast_to(part[None], (groups,) + part.shape)
    gathered = lax.all_to_all(copies, "grp", split_axis=0, concat_axis=0, tiled=True)
    return jnp.max(gathered, axis=0)


def group_gather(part, index):
    groups = lax.psum(1, "grp")
    copies = jnp.broadcast_to(part[None], (groups,) + part.shape)
    gathered = lax.all_to_all(copies, "grp", split_axis=0, concat_axis=0, tiled=True)
    return gathered.reshape((groups * part.shape[0],) + part.shape[1:])


def strided_attention(own_q, own_k, own_v, cache_kv, thread_start):
    scale = HD ** (-0.5)
    width_s = SH * HD
    rows_dev = own_q.shape[0]
    cache_here = cache_kv.shape[1]
    cols_here = cache_kv.shape[2]
    rows_all = thread_start.shape[0]
    grp = lax.axis_index("grp")

    own_kv = jnp.stack([own_k, own_v])
    plane_q = lax.all_to_all(own_q, "seq", split_axis=1, concat_axis=0, tiled=True)
    plane_kv = lax.all_to_all(own_kv, "seq", split_axis=2, concat_axis=1, tiled=True)
    return plane_q, plane_kv


BLOCK = 8


def _bias(first_key, count, starts, rows_all):
    shape = (rows_all * BLOCK, count * BLOCK)
    place = lax.broadcasted_iota(jnp.int32, shape, 0)
    spot = lax.broadcasted_iota(jnp.int32, shape, 1)
    row = place // BLOCK
    key = first_key + spot // BLOCK
    start = jnp.broadcast_to(starts[:, None], (rows_all, BLOCK)).reshape(rows_all * BLOCK, 1)
    seen = (key >= start) & (key <= CACHE + row) & (place % BLOCK == spot % BLOCK)
    return jnp.where(seen, 0.0, -jnp.inf).astype(jnp.float32)


def _head(ref, h):
    part = ref[:, :, h * HD : (h + 1) * HD].astype(jnp.float32)
    return part.reshape(part.shape[0] * BLOCK, HD).astype(jnp.bfloat16)


def _scores(q_ref, kc_ref, kw_ref, bc_ref, bw_ref, h):
    scale = HD ** (-0.5)
    q = _head(q_ref, h)
    dims = (((1,), (1,)), ((), ()))
    sc = lax.dot_general(q, _head(kc_ref, h), dims, preferred_element_type=jnp.float32)
    sw = lax.dot_general(q, _head(kw_ref, h), dims, preferred_element_type=jnp.float32)
    return sc * scale + bc_ref[...], sw * scale + bw_ref[...]


def _max_kernel(q_ref, kc_ref, kw_ref, bc_ref, bw_ref, top_ref):
    for h in range(SH):
        sc, sw = _scores(q_ref, kc_ref, kw_ref, bc_ref, bw_ref, h)
        top_ref[:, h : h + 1] = jnp.maximum(
            jnp.max(sc, axis=1, keepdims=True), jnp.max(sw, axis=1, keepdims=True)
        )


def _sum_kernel(q_ref, kc_ref, kw_ref, vc_ref, vw_ref, bc_ref, bw_ref, top_ref, acc_ref, tot_ref):
    rows = q_ref.shape[0]
    for h in range(SH):
        sc, sw = _scores(q_ref, kc_ref, kw_ref, bc_ref, bw_ref, h)
        top = top_ref[:, h : h + 1]
        ec = jnp.exp(sc - top)
        ew = jnp.exp(sw - top)
        tot = jnp.sum(ec, axis=1, keepdims=True) + jnp.sum(ew, axis=1, keepdims=True)
        acc = jnp.dot(
            ec.astype(jnp.bfloat16), _head(vc_ref, h), preferred_element_type=jnp.float32
        ) + jnp.dot(ew.astype(jnp.bfloat16), _head(vw_ref, h), preferred_element_type=jnp.float32)
        acc_ref[:, :, h * HD : (h + 1) * HD] = acc.reshape(rows, BLOCK, HD)
        tot_ref[:, :, h : h + 1] = tot.reshape(rows, BLOCK, 1)


def strided_biases(cache_here, rows_plane, thread_start):
    rows_all = thread_start.shape[0]
    grp = lax.axis_index("grp")
    starts = thread_start // STRIDE
    bias_c = _bias(grp * cache_here, cache_here, starts, rows_all)
    bias_w = _bias(CACHE + grp * rows_plane, rows_plane, starts, rows_all)
    return bias_c, bias_w


def strided_partials(all_q, plane_kv, cache_kv, offset, biases):
    width_s = SH * HD
    rows_all, cols_chunk, _ = all_q.shape
    cache_here = cache_kv.shape[1]
    rows_plane = plane_kv.shape[1]
    bias_c, bias_w = biases
    blocks = cols_chunk // BLOCK
    first = offset // BLOCK
    q_spec = pl.BlockSpec((rows_all, BLOCK, width_s), lambda j: (0, j, 0))
    kc_spec = pl.BlockSpec((None, cache_here, BLOCK, width_s), lambda j: (0, 0, first + j, 0))
    vc_spec = pl.BlockSpec((None, cache_here, BLOCK, width_s), lambda j: (1, 0, first + j, 0))
    kw_spec = pl.BlockSpec((None, rows_plane, BLOCK, width_s), lambda j: (0, 0, j, 0))
    vw_spec = pl.BlockSpec((None, rows_plane, BLOCK, width_s), lambda j: (1, 0, j, 0))
    bc_spec = pl.BlockSpec(bias_c.shape, lambda j: (0, 0))
    bw_spec = pl.BlockSpec(bias_w.shape, lambda j: (0, 0))
    top_spec = pl.BlockSpec((None, rows_all * BLOCK, SH), lambda j: (j, 0, 0))
    top_shape = jax.ShapeDtypeStruct((blocks, rows_all * BLOCK, SH), jnp.float32)
    top_part = pl.pallas_call(
        _max_kernel,
        grid=(blocks,),
        in_specs=[q_spec, kc_spec, kw_spec, bc_spec, bw_spec],
        out_specs=top_spec,
        out_shape=top_shape,
    )(all_q, cache_kv, plane_kv, bias_c, bias_w)
    top = group_max(top_part.reshape(-1, 128)).reshape(top_shape.shape)
    acc, tot = pl.pallas_call(
        _sum_kernel,
        grid=(blocks,),
        in_specs=[q_spec, kc_spec, kw_spec, vc_spec, vw_spec, bc_spec, bw_spec, top_spec],
        out_specs=[
            pl.BlockSpec((rows_all, BLOCK, width_s), lambda j: (0, j, 0)),
            pl.BlockSpec((rows_all, BLOCK, SH), lambda j: (0, j, 0)),
        ],
        out_shape=[
            jax.ShapeDtypeStruct((rows_all, cols_chunk, width_s), jnp.float32),
            jax.ShapeDtypeStruct((rows_all, cols_chunk, SH), jnp.float32),
        ],
    )(all_q, cache_kv, plane_kv, cache_kv, plane_kv, bias_c, bias_w, top)
    packed = jnp.concatenate(
        [acc.reshape(rows_all, cols_chunk * width_s), tot.reshape(rows_all, cols_chunk * SH)],
        axis=1,
    )
    return packed, rows_plane


def strided_finish(packed, rows_plane):
    width_s = SH * HD
    cols_here = (packed.shape[1]) // (width_s + SH)
    summed = lax.psum_scatter(packed, "grp", scatter_dimension=0, tiled=True)
    acc_mine = summed[:, : cols_here * width_s].reshape(rows_plane, cols_here, SH, HD)
    total_mine = summed[:, cols_here * width_s :].reshape(rows_plane, cols_here, SH)
    mixed = (acc_mine / total_mine[..., None]).astype(jnp.bfloat16)
    mixed = mixed.reshape(rows_plane, cols_here, width_s)
    return lax.all_to_all(mixed, "seq", split_axis=0, concat_axis=1, tiled=True)


CHUNKS = 2


def shards(queries, keys, values, cache_kv, thread_start):
    width_l = LH * HD
    width_s = SH * HD
    cols_here = cache_kv.shape[2]
    chunks = CHUNKS if cols_here % (CHUNKS * 16) == 0 else 1
    step = cols_here // chunks
    cols_dev = STRIDE // cols_here
    q_cols = queries[:, width_l:].reshape(-1, cols_dev, cols_here, width_s)
    k_cols = keys[:, width_l:].reshape(-1, cols_dev, cols_here, width_s)
    v_cols = values[:, width_l:].reshape(-1, cols_dev, cols_here, width_s)
    gathered = []
    for part in range(chunks):
        cut = slice(part * step, (part + 1) * step)
        gathered.append(
            strided_attention(
                q_cols[:, :, cut].reshape(-1, cols_dev * step, width_s),
                k_cols[:, :, cut].reshape(-1, cols_dev * step, width_s),
                v_cols[:, :, cut].reshape(-1, cols_dev * step, width_s),
                cache_kv,
                thread_start,
            )
        )
    planes = tuple(g[0] for g in gathered)
    gathered = [[group_gather(g[0], part), g[1]] for part, g in enumerate(gathered)]
    gathered[0][0], planes = lax.optimization_barrier((gathered[0][0], planes))
    biases = strided_biases(cache_kv.shape[1], gathered[0][1].shape[1], thread_start)
    pieces = []
    local_in = (queries[:, :width_l], keys[:, :width_l], values[:, :width_l])
    for part in range(chunks):
        packed, rows_plane = strided_partials(*gathered[part], cache_kv, part * step, biases)
        if part + 1 < chunks:
            packed, gathered[part + 1] = lax.optimization_barrier((packed, gathered[part + 1]))
        else:
            packed, local_in = lax.optimization_barrier((packed, local_in))
        pieces.append(strided_finish(packed, rows_plane))
    local_out = local_attention(*local_in)
    strided_out = jnp.concatenate(
        [p.reshape(-1, cols_dev, step, width_s) for p in pieces], axis=2
    ).reshape(-1, width_s)
    return jnp.concatenate([local_out.astype(jnp.bfloat16), strided_out], axis=1)


def solution(mesh):
    placed = (
        P(("grp", "seq"), None),
        P(("grp", "seq"), None),
        P(("grp", "seq"), None),
        P(None, "grp", "seq", None),
        P(),
    )
    return jax.shard_map(
        shards, mesh=mesh, in_specs=placed, out_specs=P(("grp", "seq"), None), check_vma=False
    )
```

```python
import jax
import jax.numpy as jnp
from jax import lax
from jax.experimental import pallas as pl
from jax.sharding import PartitionSpec as P

LH = 8
SH = 8
HD = 64
STRIDE = 1024
CACHE = 128


def local_attention(q_part, k_part, v_part):
    scale = HD ** (-0.5)
    tok = q_part.shape[0]
    rows_dev = tok // STRIDE
    block = min(512, STRIDE)
    per_row = STRIDE // block
    q_blocks = q_part.reshape(tok // block, block, LH, HD)
    k_rows = k_part.reshape(rows_dev, STRIDE, LH, HD)
    v_rows = v_part.reshape(rows_dev, STRIDE, LH, HD)
    key_place = jnp.arange(STRIDE, dtype=jnp.int32)

    def one_block(index):
        row_index = index // per_row
        first = index % per_row * block
        query = lax.dynamic_index_in_dim(q_blocks, index, 0, keepdims=False)
        key_row = lax.dynamic_index_in_dim(k_rows, row_index, 0, keepdims=False)
        value_row = lax.dynamic_index_in_dim(v_rows, row_index, 0, keepdims=False)
        scores = (
            jnp.einsum("qhd,khd->hqk", query, key_row, preferred_element_type=jnp.float32) * scale
        )
        causal = (first + jnp.arange(block, dtype=jnp.int32))[:, None] >= key_place[None, :]
        scores = jnp.where(causal[None], scores, -jnp.inf)
        top = jnp.max(scores, axis=-1, keepdims=True)
        expo = jnp.exp(scores - top)
        total = jnp.sum(expo, axis=-1)
        mixed = jnp.einsum(
            "hqk,khd->qhd", expo.astype(jnp.bfloat16), value_row, preferred_element_type=jnp.float32
        )
        return (mixed / jnp.transpose(total)[:, :, None]).reshape(block, LH * HD)

    result = [one_block(index) for index in range(tok // block)]
    return jnp.concatenate(result, axis=0)


def group_max(part):
    groups = lax.psum(1, "grp")
    copies = jnp.broadcast_to(part[None], (groups,) + part.shape)
    gathered = lax.all_to_all(copies, "grp", split_axis=0, concat_axis=0, tiled=True)
    return jnp.max(gathered, axis=0)


def strided_attention(own_q, own_k, own_v, cache_kv, thread_start):
    scale = HD ** (-0.5)
    width_s = SH * HD
    rows_dev = own_q.shape[0]
    cache_here = cache_kv.shape[1]
    cols_here = cache_kv.shape[2]
    rows_all = thread_start.shape[0]
    grp = lax.axis_index("grp")

    own_kv = jnp.stack([own_k, own_v])
    plane_q = lax.all_to_all(own_q, "seq", split_axis=1, concat_axis=0, tiled=True)
    plane_kv = lax.all_to_all(own_kv, "seq", split_axis=2, concat_axis=1, tiled=True)
    return plane_q, plane_kv


BLOCK = 8


def _bias(first_key, count, starts, rows_all):
    shape = (rows_all * BLOCK, count * BLOCK)
    place = lax.broadcasted_iota(jnp.int32, shape, 0)
    spot = lax.broadcasted_iota(jnp.int32, shape, 1)
    row = place // BLOCK
    key = first_key + spot // BLOCK
    start = jnp.broadcast_to(starts[:, None], (rows_all, BLOCK)).reshape(rows_all * BLOCK, 1)
    seen = (key >= start) & (key <= CACHE + row) & (place % BLOCK == spot % BLOCK)
    return jnp.where(seen, 0.0, -jnp.inf).astype(jnp.float32)


def _head(ref, h):
    part = ref[:, :, h * HD : (h + 1) * HD].astype(jnp.float32)
    return part.reshape(part.shape[0] * BLOCK, HD).astype(jnp.bfloat16)


def _scores(q_ref, kc_ref, kw_ref, bc_ref, bw_ref, h):
    scale = HD ** (-0.5)
    q = _head(q_ref, h)
    dims = (((1,), (1,)), ((), ()))
    sc = lax.dot_general(q, _head(kc_ref, h), dims, preferred_element_type=jnp.float32)
    sw = lax.dot_general(q, _head(kw_ref, h), dims, preferred_element_type=jnp.float32)
    return sc * scale + bc_ref[...], sw * scale + bw_ref[...]


def _max_kernel(q_ref, kc_ref, kw_ref, bc_ref, bw_ref, top_ref):
    for h in range(SH):
        sc, sw = _scores(q_ref, kc_ref, kw_ref, bc_ref, bw_ref, h)
        top_ref[:, h : h + 1] = jnp.maximum(
            jnp.max(sc, axis=1, keepdims=True), jnp.max(sw, axis=1, keepdims=True)
        )


def _sum_kernel(q_ref, kc_ref, kw_ref, vc_ref, vw_ref, bc_ref, bw_ref, top_ref, acc_ref, tot_ref):
    rows = q_ref.shape[0]
    for h in range(SH):
        sc, sw = _scores(q_ref, kc_ref, kw_ref, bc_ref, bw_ref, h)
        top = top_ref[:, h : h + 1]
        ec = jnp.exp(sc - top)
        ew = jnp.exp(sw - top)
        tot = jnp.sum(ec, axis=1, keepdims=True) + jnp.sum(ew, axis=1, keepdims=True)
        acc = jnp.dot(
            ec.astype(jnp.bfloat16), _head(vc_ref, h), preferred_element_type=jnp.float32
        ) + jnp.dot(ew.astype(jnp.bfloat16), _head(vw_ref, h), preferred_element_type=jnp.float32)
        acc_ref[:, :, h * HD : (h + 1) * HD] = acc.reshape(rows, BLOCK, HD)
        tot_ref[:, :, h : h + 1] = tot.reshape(rows, BLOCK, 1)


def strided_biases(cache_here, rows_plane, thread_start):
    rows_all = thread_start.shape[0]
    grp = lax.axis_index("grp")
    starts = thread_start // STRIDE
    bias_c = _bias(grp * cache_here, cache_here, starts, rows_all)
    bias_w = _bias(CACHE + grp * rows_plane, rows_plane, starts, rows_all)
    return bias_c, bias_w


def strided_partials(all_q, plane_kv, cache_kv, offset, biases):
    width_s = SH * HD
    rows_all, cols_chunk, _ = all_q.shape
    cache_here = cache_kv.shape[1]
    rows_plane = plane_kv.shape[1]
    bias_c, bias_w = biases
    blocks = cols_chunk // BLOCK
    first = offset // BLOCK
    q_spec = pl.BlockSpec((rows_all, BLOCK, width_s), lambda j: (0, j, 0))
    kc_spec = pl.BlockSpec((None, cache_here, BLOCK, width_s), lambda j: (0, 0, first + j, 0))
    vc_spec = pl.BlockSpec((None, cache_here, BLOCK, width_s), lambda j: (1, 0, first + j, 0))
    kw_spec = pl.BlockSpec((None, rows_plane, BLOCK, width_s), lambda j: (0, 0, j, 0))
    vw_spec = pl.BlockSpec((None, rows_plane, BLOCK, width_s), lambda j: (1, 0, j, 0))
    bc_spec = pl.BlockSpec(bias_c.shape, lambda j: (0, 0))
    bw_spec = pl.BlockSpec(bias_w.shape, lambda j: (0, 0))
    top_spec = pl.BlockSpec((None, rows_all * BLOCK, SH), lambda j: (j, 0, 0))
    top_shape = jax.ShapeDtypeStruct((blocks, rows_all * BLOCK, SH), jnp.float32)
    top_part = pl.pallas_call(
        _max_kernel,
        grid=(blocks,),
        in_specs=[q_spec, kc_spec, kw_spec, bc_spec, bw_spec],
        out_specs=top_spec,
        out_shape=top_shape,
    )(all_q, cache_kv, plane_kv, bias_c, bias_w)
    top = group_max(top_part.reshape(-1, 128)).reshape(top_shape.shape)
    acc, tot = pl.pallas_call(
        _sum_kernel,
        grid=(blocks,),
        in_specs=[q_spec, kc_spec, kw_spec, vc_spec, vw_spec, bc_spec, bw_spec, top_spec],
        out_specs=[
            pl.BlockSpec((rows_all, BLOCK, width_s), lambda j: (0, j, 0)),
            pl.BlockSpec((rows_all, BLOCK, SH), lambda j: (0, j, 0)),
        ],
        out_shape=[
            jax.ShapeDtypeStruct((rows_all, cols_chunk, width_s), jnp.float32),
            jax.ShapeDtypeStruct((rows_all, cols_chunk, SH), jnp.float32),
        ],
    )(all_q, cache_kv, plane_kv, cache_kv, plane_kv, bias_c, bias_w, top)
    packed = jnp.concatenate(
        [acc.reshape(rows_all, cols_chunk * width_s), tot.reshape(rows_all, cols_chunk * SH)],
        axis=1,
    )
    return packed, rows_plane


def strided_finish(packed, rows_plane):
    width_s = SH * HD
    cols_here = (packed.shape[1]) // (width_s + SH)
    summed = lax.psum_scatter(packed, "grp", scatter_dimension=0, tiled=True)
    acc_mine = summed[:, : cols_here * width_s].reshape(rows_plane, cols_here, SH, HD)
    total_mine = summed[:, cols_here * width_s :].reshape(rows_plane, cols_here, SH)
    mixed = (acc_mine / total_mine[..., None]).astype(jnp.bfloat16)
    mixed = mixed.reshape(rows_plane, cols_here, width_s)
    return lax.all_to_all(mixed, "seq", split_axis=0, concat_axis=1, tiled=True)


CHUNKS = 4


def shards(queries, keys, values, cache_kv, thread_start):
    width_l = LH * HD
    width_s = SH * HD
    cols_here = cache_kv.shape[2]
    chunks = CHUNKS if cols_here % (CHUNKS * 16) == 0 else 1
    step = cols_here // chunks
    cols_dev = STRIDE // cols_here
    q_cols = queries[:, width_l:].reshape(-1, cols_dev, cols_here, width_s)
    k_cols = keys[:, width_l:].reshape(-1, cols_dev, cols_here, width_s)
    v_cols = values[:, width_l:].reshape(-1, cols_dev, cols_here, width_s)
    gathered = []
    for part in range(chunks):
        cut = slice(part * step, (part + 1) * step)
        gathered.append(
            strided_attention(
                q_cols[:, :, cut].reshape(-1, cols_dev * step, width_s),
                k_cols[:, :, cut].reshape(-1, cols_dev * step, width_s),
                v_cols[:, :, cut].reshape(-1, cols_dev * step, width_s),
                cache_kv,
                thread_start,
            )
        )
    planes = tuple(g[0] for g in gathered)
    gathered = [[lax.all_gather(g[0], "grp", axis=0, tiled=True), g[1]] for g in gathered]
    gathered[0][0], planes = lax.optimization_barrier((gathered[0][0], planes))
    biases = strided_biases(cache_kv.shape[1], gathered[0][1].shape[1], thread_start)
    pieces = []
    local_in = (queries[:, :width_l], keys[:, :width_l], values[:, :width_l])
    for part in range(chunks):
        packed, rows_plane = strided_partials(*gathered[part], cache_kv, part * step, biases)
        if part + 1 < chunks:
            packed, gathered[part + 1] = lax.optimization_barrier((packed, gathered[part + 1]))
        else:
            packed, local_in = lax.optimization_barrier((packed, local_in))
        pieces.append(strided_finish(packed, rows_plane))
    local_out = local_attention(*local_in)
    strided_out = jnp.concatenate(
        [p.reshape(-1, cols_dev, step, width_s) for p in pieces], axis=2
    ).reshape(-1, width_s)
    return jnp.concatenate([local_out.astype(jnp.bfloat16), strided_out], axis=1)


def solution(mesh):
    placed = (
        P(("grp", "seq"), None),
        P(("grp", "seq"), None),
        P(("grp", "seq"), None),
        P(None, "grp", "seq", None),
        P(),
    )
    return jax.shard_map(
        shards, mesh=mesh, in_specs=placed, out_specs=P(("grp", "seq"), None), check_vma=False
    )
```
